512 devices in a mesh: clip: 16 (over y, z_hi), seq: 32 (over x, z_lo, core).
Axes of the slice: x: 4, y: 4, z: 16 (z_hi: 4, z_lo: 4; z = z_hi * 4 + z_lo), core: 2. Of those that a mesh axis runs over, the one named last changes fastest.
Arguments:
- frames_in: bfloat16 [512, 256, 1152], P(('clip', 'seq')), parts along dimension 0, may hold values from -6 to 6
- modulation: float32 [48, 1152], P('clip'), parts along dimension 0, may hold values from -3 to 3
- self_proj: bfloat16 [1152, 1728], P(None, 'seq'), may hold values from -0.1875 to 0.1875
- self_out: bfloat16 [576, 1152], P(None, 'seq'), may hold values from -0.25 to 0.25
- cross_query: bfloat16 [1152, 576], P(None, 'seq'), may hold values from -0.1875 to 0.1875
- cross_keyval: bfloat16 [1152, 1152], P(None, 'seq'), may hold values from -0.1875 to 0.1875
- cross_out: bfloat16 [576, 1152], P(None, 'seq'), may hold values from -0.25 to 0.25
- text_bank: bfloat16 [32, 256, 1152], P('seq'), may hold values from -6 to 6
- prompt_pick: int32 [16], P('clip'), parts along dimension 0, may hold values from 0 to 31
- text_lengths: int32 [32], replicated, may hold values from 32 to 256
Outputs:
- frames_out: bfloat16 [512, 256, 1152], P(('clip', 'seq')), parts along dimension 0
The draws below stay inside these ranges and needn't reach their ends.
There are 16 independent parts, one for each index of `clip`. The reference program is written for one: setup_inputs(seed, part) draws one part's arguments, and reference() takes and returns one part's arrays. A program takes and returns all parts, laid end to end along the dimension named above; an argument that names none is the same for every part. Nothing has to cross between parts.
All inputs are finite; a program needn't handle non-finite values.
Results may differ from the reference program's by a relative error of at most 0.006.
Values may be sent and summed in bfloat16 or wider, within the bound.
No kernel may reach another device: no remote copies, remote signals or barrier semaphores. Data moves between devices by JAX's collectives and lax.ppermute only.
A program may use at most 64 MiB of HBM per device.

```python
import math
import jax
import jax.numpy as jnp
from jax import lax

WIDTH = 1152
HEAD_DIM = 72
HEADS_WIN = 8
ATTN = 576
FRAMES = 32
PIXELS = 256
TXT = 256
PROMPTS = 32


def set_ends(result, own_key, smallest, high):
    longest = result.shape.index(max(result.shape))
    spots = []
    for shift in (0, 1):
        where = [jax.random.randint(jax.random.fold_in(own_key, axis), (), 0, length) for axis, length in enumerate(result.shape)]
        where[longest] = (where[longest] + shift) % result.shape[longest]
        spots.append(tuple(where))
    return result.at[spots[0]].set(smallest).at[spots[1]].set(high)


def level_of(own_key, dims, split, least, top_value):
    def one(dim, parts):
        heights = jax.random.uniform(jax.random.fold_in(jax.random.fold_in(own_key, 6), dim), (parts,), jnp.float32, least / len(split), top_value / len(split))
        return jnp.repeat(jnp.exp(heights), dims[dim] // parts).reshape((-1,) + (1,) * (len(dims) - dim - 1))

    loudness = one(*split[0])
    for cut in split[1:]:
        loudness = loudness * one(*cut)
    return loudness


def noise(own_key, shape, scale, bound, cuts=(), kind=jnp.bfloat16):
    factor_of = level_of(own_key, shape, cuts, -0.22, 0.18) if cuts else 1.0
    entries = jax.random.normal(own_key, shape, jnp.float32) * scale * factor_of
    return jnp.minimum(jnp.maximum(entries, -bound), bound).astype(kind)


def setup_inputs(seed: int = 0, part: int = 0) -> dict:
    splits = jax.random.split(jax.random.key(seed), 11)
    own_keys = jax.random.split(jax.random.fold_in(splits[10], part), 11)
    return {
        "frames_in": noise(own_keys[0], (FRAMES, PIXELS, WIDTH), 1.0, 6.0, ((0, 32),)),
        "modulation": noise(own_keys[1], (3, WIDTH), 0.5, 3.0, (), jnp.float32),
        "self_proj": noise(splits[2], (WIDTH, 3 * ATTN), WIDTH ** -0.5, 0.1875, ((1, 32),)),
        "self_out": noise(splits[3], (ATTN, WIDTH), ATTN ** -0.5, 0.25, ((1, 32),)),
        "cross_query": noise(splits[4], (WIDTH, ATTN), WIDTH ** -0.5, 0.1875, ((1, 32),)),
        "cross_keyval": noise(splits[5], (WIDTH, 2 * ATTN), WIDTH ** -0.5, 0.1875, ((1, 32),)),
        "cross_out": noise(splits[6], (ATTN, WIDTH), ATTN ** -0.5, 0.25, ((1, 32),)),
        "text_bank": noise(splits[7], (PROMPTS, TXT, WIDTH), 1.0, 6.0, ((0, 32),)),
        "prompt_pick": jax.random.randint(own_keys[8], (1,), 0, PROMPTS).astype(jnp.int32),
        "text_lengths": set_ends(jax.random.randint(splits[9], (PROMPTS,), TXT // 8, TXT + 1), jax.random.fold_in(splits[9], 1), TXT // 8, TXT).astype(jnp.int32),
    }


EPS = 1e-06

def layer_norm(values):
    mean = lax.optimization_barrier(jnp.mean(values, axis=-1, keepdims=True))
    centred = values - mean
    spread = lax.optimization_barrier(jnp.mean(centred * centred, axis=-1, keepdims=True))
    return centred * lax.rsqrt(spread + EPS)

def head_norm(values, heads):
    shaped = values.reshape(values.shape[:-1] + (heads, values.shape[-1] // heads))
    power = lax.optimization_barrier(jnp.mean(shaped * shaped, axis=-1, keepdims=True))
    return shaped * lax.rsqrt(power + EPS)

def reference(frames_in, modulation, self_proj, self_out, cross_query, cross_keyval, cross_out, text_bank, prompt_pick, text_lengths):
    heads = HEADS_WIN
    attn = heads * HEAD_DIM
    scale_q = 1.0 / math.sqrt(HEAD_DIM)
    tokens = frames_in.astype(jnp.float32)
    normed = (layer_norm(tokens) * (1.0 + modulation[1]) + modulation[0]).astype(jnp.bfloat16)
    qkv = jnp.dot(normed.reshape(-1, WIDTH), self_proj, preferred_element_type=jnp.float32).astype(jnp.bfloat16)
    qkv = qkv.reshape(FRAMES, PIXELS, 3 * attn)
    query = (head_norm(qkv[..., :attn].astype(jnp.float32), heads) * scale_q).astype(jnp.bfloat16)
    key = head_norm(qkv[..., attn:2 * attn].astype(jnp.float32), heads).astype(jnp.bfloat16)
    value = qkv[..., 2 * attn:].reshape(FRAMES, PIXELS, heads, HEAD_DIM)
    scores = jnp.einsum('fphd,gphd->phfg', query.astype(jnp.float32), key.astype(jnp.float32))
    weights = jnp.exp(scores)
    total = lax.optimization_barrier(jnp.sum(weights, axis=-1))
    probs = lax.optimization_barrier(weights.astype(jnp.bfloat16)).astype(jnp.float32)
    mixed = jnp.einsum('phfg,gphd->fphd', probs, value.astype(jnp.float32))
    attended = (mixed / jnp.transpose(total, (2, 0, 1))[..., None]).astype(jnp.bfloat16).reshape(-1, attn)
    self_term = jnp.dot(attended, self_out, preferred_element_type=jnp.float32)
    after_self = (tokens.reshape(-1, WIDTH) + modulation[2] * self_term).astype(jnp.bfloat16)
    pick = prompt_pick[0]
    memory = lax.dynamic_index_in_dim(text_bank, pick, 0, keepdims=False)
    keyval = jnp.dot(memory, cross_keyval, preferred_element_type=jnp.float32).astype(jnp.bfloat16)
    text_key = head_norm(keyval[:, :attn].astype(jnp.float32), heads).astype(jnp.bfloat16)
    text_value = keyval[:, attn:].reshape(TXT, heads, HEAD_DIM)
    length = lax.dynamic_index_in_dim(text_lengths, pick, 0, keepdims=False)
    live = jnp.arange(TXT, dtype=jnp.int32) < length
    text_query = jnp.dot(after_self, cross_query, preferred_element_type=jnp.float32)
    text_query = (head_norm(text_query, heads) * scale_q).astype(jnp.bfloat16)

    def cross_block(block):
        block_scores = jnp.einsum('phd,lhd->phl', block.astype(jnp.float32), text_key.astype(jnp.float32))
        block_weights = jnp.where(live, jnp.exp(block_scores), 0.0)
        block_total = lax.optimization_barrier(jnp.sum(block_weights, axis=-1))
        block_probs = lax.optimization_barrier(block_weights.astype(jnp.bfloat16)).astype(jnp.float32)
        block_mix = jnp.einsum('phl,lhd->phd', block_probs, text_value.astype(jnp.float32))
        return (block_mix / block_total[..., None]).astype(jnp.bfloat16)
    crossed = lax.map(cross_block, text_query.reshape(FRAMES, PIXELS, heads, HEAD_DIM)).reshape(-1, attn)
    cross_term = jnp.dot(crossed, cross_out, preferred_element_type=jnp.float32)
    frames_out = (after_self.astype(jnp.float32) + cross_term).astype(jnp.bfloat16)
    return frames_out.reshape(FRAMES, PIXELS, WIDTH)
```

```python
import math

import jax
import jax.numpy as jnp
from jax import lax
from jax.sharding import PartitionSpec as P

HEAD_DIM = 72


EPS = 1e-06


def layer_norm(values):
    mean = jnp.mean(values, axis=-1, keepdims=True)
    centred = values - mean
    spread = jnp.mean(centred * centred, axis=-1, keepdims=True)
    return centred * lax.rsqrt(spread + EPS)


def head_norm(values, heads):
    shaped = values.reshape(values.shape[:-1] + (heads, values.shape[-1] // heads))
    power = jnp.mean(shaped * shaped, axis=-1, keepdims=True)
    return shaped * lax.rsqrt(power + EPS)


def temporal_attention(qkv, heads, attn, scale_q):
    frames, patches = (qkv.shape[0], qkv.shape[1])
    query = (head_norm(qkv[..., :attn].astype(jnp.float32), heads) * scale_q).astype(jnp.bfloat16)
    key = head_norm(qkv[..., attn : 2 * attn].astype(jnp.float32), heads).astype(jnp.bfloat16)
    value = qkv[..., 2 * attn :].reshape(frames, patches, heads, attn // heads)
    scores = jnp.einsum("fphd,gphd->phfg", query, key, preferred_element_type=jnp.float32)
    weights = jnp.exp(scores)
    total = jnp.sum(weights, axis=-1)
    probs = weights.astype(jnp.bfloat16)
    mixed = jnp.einsum("phfg,gphd->fphd", probs, value, preferred_element_type=jnp.float32)
    attended = mixed / jnp.transpose(total, (2, 0, 1))[..., None]
    return attended.astype(jnp.bfloat16).reshape(frames, patches, attn)


def gather_rows(blocks, axis):
    packed = jnp.concatenate(blocks, axis=0)
    full = lax.all_gather(packed, axis, axis=0, tiled=False)
    out, start = [], 0
    for b in blocks:
        out.append(full[:, start : start + b.shape[0], :])
        start += b.shape[0]
    return out


def project(x, gathered):
    count, cols, _ = gathered.shape
    y = jnp.einsum("tk,sck->tsc", x, gathered, preferred_element_type=jnp.float32)
    return y.reshape(x.shape[0], count * cols)


def per_device(
    frames_in,
    modulation,
    self_proj,
    self_out,
    cross_query,
    cross_keyval,
    cross_out,
    text_bank,
    prompt_pick,
    text_lengths,
):
    count = lax.axis_size("seq")
    frame_rows, pixels, width = frames_in.shape
    attn = self_out.shape[0]
    heads = attn // HEAD_DIM
    scale_q = 1.0 / math.sqrt(HEAD_DIM)
    pix_dev = pixels // count
    frames = frame_rows * count
    text_len = text_bank.shape[1]
    txt_dev = text_len // count

    (proj_g,) = gather_rows([self_proj.T], "seq")
    query_g, keyval_g, so_g, co_g = gather_rows(
        [
            cross_query.T,
            cross_keyval.T,
            self_out.T.reshape(-1, width),
            cross_out.T.reshape(-1, width),
        ],
        "seq",
    )

    tokens = frames_in.astype(jnp.float32)
    normed = (layer_norm(tokens) * (1.0 + modulation[1]) + modulation[0]).astype(jnp.bfloat16)
    send = jnp.concatenate(
        [
            normed.reshape(count, pix_dev, width),
            text_bank[0].reshape(count, txt_dev, width),
        ],
        axis=1,
    )
    recv = lax.all_to_all(send, "seq", 0, 0, tiled=True)
    switched = recv[:, :pix_dev, :]
    pick = prompt_pick[0]
    memory_rows = lax.dynamic_index_in_dim(recv[:, pix_dev:, :], pick, 0, keepdims=False)

    flat_pix = switched.reshape(-1, width)
    qkv = project(flat_pix, proj_g).astype(jnp.bfloat16)
    qkv = qkv.reshape(frames, pix_dev, 3 * attn)
    attended = temporal_attention(qkv, heads, attn, scale_q)

    keyval_rows = project(memory_rows, keyval_g).astype(jnp.bfloat16)
    key_rows = head_norm(keyval_rows[:, :attn].astype(jnp.float32), heads).astype(jnp.bfloat16)
    kv_rows = jnp.concatenate([key_rows.reshape(txt_dev, attn), keyval_rows[:, attn:]], axis=1)

    send2 = jnp.concatenate(
        [
            attended.reshape(count, -1),
            jnp.broadcast_to(kv_rows.reshape(1, -1), (count, txt_dev * 2 * attn)),
        ],
        axis=1,
    )
    recv2 = lax.all_to_all(send2, "seq", 0, 0, tiled=True)
    returned = recv2[:, : pix_dev * attn].reshape(pixels, attn)
    keyval = recv2[:, pix_dev * attn :].reshape(text_len, 2 * attn)

    out_self = so_g.reshape(width, attn)
    out_cross = co_g.reshape(width, attn)
    self_term = jnp.einsum("ta,ca->tc", returned, out_self, preferred_element_type=jnp.float32)
    after_self = (tokens.reshape(-1, width) + modulation[2] * self_term).astype(jnp.bfloat16)

    text_key = keyval[:, :attn].reshape(text_len, heads, HEAD_DIM)
    text_value = keyval[:, attn:].reshape(text_len, heads, HEAD_DIM)
    slots = jnp.arange(text_lengths.shape[0], dtype=jnp.int32)
    length = jnp.sum(jnp.where(slots == pick, text_lengths, 0))
    live = jnp.arange(text_len, dtype=jnp.int32) < length
    text_query = project(after_self, query_g)
    text_query = (head_norm(text_query, heads) * scale_q).astype(jnp.bfloat16)
    cross_scores = jnp.einsum(
        "thd,lhd->thl", text_query, text_key, preferred_element_type=jnp.float32
    )
    cross_weights = jnp.where(live, jnp.exp(cross_scores), 0.0)
    cross_total = jnp.sum(cross_weights, axis=-1)
    cross_probs = cross_weights.astype(jnp.bfloat16)
    cross_mix = jnp.einsum(
        "thl,lhd->thd", cross_probs, text_value, preferred_element_type=jnp.float32
    )
    crossed = (cross_mix / cross_total[..., None]).astype(jnp.bfloat16).reshape(-1, attn)
    cross_term = jnp.einsum("ta,ca->tc", crossed, out_cross, preferred_element_type=jnp.float32)
    frames_out = (after_self.astype(jnp.float32) + cross_term).astype(jnp.bfloat16)
    return frames_out.reshape(frame_rows, pixels, width)


def solution(mesh):
    placed = (
        P(("clip", "seq"), None, None),
        P("clip", None),
        P(None, "seq"),
        P(None, "seq"),
        P(None, "seq"),
        P(None, "seq"),
        P(None, "seq"),
        P("seq", None, None),
        P("clip"),
        P(),
    )
    return jax.shard_map(
        per_device,
        mesh=mesh,
        in_specs=placed,
        out_specs=P(("clip", "seq"), None, None),
        check_vma=False,
    )
```

```python
import math

import jax
import jax.numpy as jnp
from jax import lax
from jax.sharding import PartitionSpec as P

HEAD_DIM = 72


EPS = 1e-06


def layer_norm(values):
    mean = jnp.mean(values, axis=-1, keepdims=True)
    centred = values - mean
    spread = jnp.mean(centred * centred, axis=-1, keepdims=True)
    return centred * lax.rsqrt(spread + EPS)


def head_norm(values, heads):
    shaped = values.reshape(values.shape[:-1] + (heads, values.shape[-1] // heads))
    power = jnp.mean(shaped * shaped, axis=-1, keepdims=True)
    return shaped * lax.rsqrt(power + EPS)


def temporal_attention(qkv, heads, attn, scale_q):
    frames, patches = (qkv.shape[0], qkv.shape[1])
    query = (head_norm(qkv[..., :attn].astype(jnp.float32), heads) * scale_q).astype(jnp.bfloat16)
    key = head_norm(qkv[..., attn : 2 * attn].astype(jnp.float32), heads).astype(jnp.bfloat16)
    value = qkv[..., 2 * attn :].reshape(frames, patches, heads, attn // heads)
    scores = jnp.einsum("fphd,gphd->phfg", query, key, preferred_element_type=jnp.float32)
    weights = jnp.exp(scores)
    total = jnp.sum(weights, axis=-1)
    probs = weights.astype(jnp.bfloat16)
    mixed = jnp.einsum("phfg,gphd->fphd", probs, value, preferred_element_type=jnp.float32)
    attended = mixed / jnp.transpose(total, (2, 0, 1))[..., None]
    return attended.astype(jnp.bfloat16).reshape(frames, patches, attn)


def pack_rows(pieces):
    total = sum(p.shape[1] for p in pieces)
    eye = jnp.eye(total, dtype=pieces[0].dtype)
    packed, start = None, 0
    for p in pieces:
        part = jnp.einsum(
            "rc,kc->rk", eye[:, start : start + p.shape[1]], p, preferred_element_type=jnp.float32
        )
        packed = part if packed is None else packed + part
        start += p.shape[1]
    return packed.astype(pieces[0].dtype)


def project(x, gathered):
    count, cols, _ = gathered.shape
    y = jnp.einsum("tk,sck->tsc", x, gathered, preferred_element_type=jnp.float32)
    return y.reshape(x.shape[0], count * cols)


def project_block(x, gathered, start, cols):
    count, rows, _ = gathered.shape
    y = jnp.einsum("tk,sck->tsc", x, gathered, preferred_element_type=jnp.float32)
    return y[:, :, start : start + cols].reshape(x.shape[0], count * cols)


def per_device(
    frames_in,
    modulation,
    self_proj,
    self_out,
    cross_query,
    cross_keyval,
    cross_out,
    text_bank,
    prompt_pick,
    text_lengths,
):
    count = lax.axis_size("seq")
    frame_rows, pixels, width = frames_in.shape
    attn = self_out.shape[0]
    heads = attn // HEAD_DIM
    scale_q = 1.0 / math.sqrt(HEAD_DIM)
    pix_dev = pixels // count
    frames = frame_rows * count
    text_len = text_bank.shape[1]
    txt_dev = text_len // count

    outs_pair = jnp.concatenate([self_out, cross_out], axis=0)
    sizes = (self_proj.shape[1], cross_keyval.shape[1], cross_query.shape[1], outs_pair.shape[1])
    packed = pack_rows([self_proj, cross_keyval, cross_query, outs_pair])
    gathered = lax.all_gather(packed, "seq", axis=0, tiled=False)
    kv_at = sizes[0]
    q_at = kv_at + sizes[1]
    outs_at = q_at + sizes[2]
    query_g = gathered[:, q_at : q_at + sizes[2], :]
    outs_g = gathered[:, outs_at : outs_at + sizes[3], :]

    tokens = frames_in.astype(jnp.float32)
    normed = (layer_norm(tokens) * (1.0 + modulation[1]) + modulation[0]).astype(jnp.bfloat16)
    send = jnp.concatenate(
        [
            normed.reshape(count, pix_dev, width),
            text_bank[0].reshape(count, txt_dev, width),
        ],
        axis=1,
    )
    recv = lax.all_to_all(send, "seq", 0, 0, tiled=True)
    switched = recv[:, :pix_dev, :]
    pick = prompt_pick[0]
    memory_rows = lax.dynamic_index_in_dim(recv[:, pix_dev:, :], pick, 0, keepdims=False)

    flat_pix = switched.reshape(-1, width)
    qkv = project_block(flat_pix, gathered, 0, sizes[0]).astype(jnp.bfloat16)
    qkv = qkv.reshape(frames, pix_dev, 3 * attn)
    attended = temporal_attention(qkv, heads, attn, scale_q)

    keyval_rows = project_block(memory_rows, gathered, kv_at, sizes[1]).astype(jnp.bfloat16)
    key_rows = head_norm(keyval_rows[:, :attn].astype(jnp.float32), heads).astype(jnp.bfloat16)
    kv_rows = jnp.concatenate([key_rows.reshape(txt_dev, attn), keyval_rows[:, attn:]], axis=1)

    send2 = jnp.concatenate(
        [
            attended.reshape(count, -1),
            jnp.broadcast_to(kv_rows.reshape(1, -1), (count, txt_dev * 2 * attn)),
        ],
        axis=1,
    )
    recv2 = lax.all_to_all(send2, "seq", 0, 0, tiled=True)
    returned = recv2[:, : pix_dev * attn].reshape(pixels, attn)
    keyval = recv2[:, pix_dev * attn :].reshape(text_len, 2 * attn)

    out_self = outs_g[:, :, :attn].reshape(-1, attn)
    out_cross = outs_g[:, :, attn:].reshape(-1, attn)
    self_term = jnp.einsum("ta,ca->tc", returned, out_self, preferred_element_type=jnp.float32)
    after_self = (tokens.reshape(-1, width) + modulation[2] * self_term).astype(jnp.bfloat16)

    text_key = keyval[:, :attn].reshape(text_len, heads, HEAD_DIM)
    text_value = keyval[:, attn:].reshape(text_len, heads, HEAD_DIM)
    slots = jnp.arange(text_lengths.shape[0], dtype=jnp.int32)
    length = jnp.sum(jnp.where(slots == pick, text_lengths, 0))
    live = jnp.arange(text_len, dtype=jnp.int32) < length
    text_query = project(after_self, query_g)
    text_query = (head_norm(text_query, heads) * scale_q).astype(jnp.bfloat16)
    cross_scores = jnp.einsum(
        "thd,lhd->thl", text_query, text_key, preferred_element_type=jnp.float32
    )
    cross_weights = jnp.where(live, jnp.exp(cross_scores), 0.0)
    cross_total = jnp.sum(cross_weights, axis=-1)
    cross_probs = cross_weights.astype(jnp.bfloat16)
    cross_mix = jnp.einsum(
        "thl,lhd->thd", cross_probs, text_value, preferred_element_type=jnp.float32
    )
    crossed = (cross_mix / cross_total[..., None]).astype(jnp.bfloat16).reshape(-1, attn)
    cross_term = jnp.einsum("ta,ca->tc", crossed, out_cross, preferred_element_type=jnp.float32)
    frames_out = (after_self.astype(jnp.float32) + cross_term).astype(jnp.bfloat16)
    return frames_out.reshape(frame_rows, pixels, width)


def solution(mesh):
    placed = (
        P(("clip", "seq"), None, None),
        P("clip", None),
        P(None, "seq"),
        P(None, "seq"),
        P(None, "seq"),
        P(None, "seq"),
        P(None, "seq"),
        P("seq", None, None),
        P("clip"),
        P(),
    )
    return jax.shard_map(
        per_device,
        mesh=mesh,
        in_specs=placed,
        out_specs=P(("clip", "seq"), None, None),
        check_vma=False,
    )
```

```python
import math

import jax
import jax.numpy as jnp
from jax import lax
from jax.sharding import PartitionSpec as P

HEAD_DIM = 72


EPS = 1e-06


def layer_norm(values):
    mean = jnp.mean(values, axis=-1, keepdims=True)
    centred = values - mean
    spread = jnp.mean(centred * centred, axis=-1, keepdims=True)
    return centred * lax.rsqrt(spread + EPS)


def head_norm(values, heads):
    shaped = values.reshape(values.shape[:-1] + (heads, values.shape[-1] // heads))
    power = jnp.mean(shaped * shaped, axis=-1, keepdims=True)
    return shaped * lax.rsqrt(power + EPS)


def temporal_attention(qkv, heads, attn, scale_q):
    frames, patches = (qkv.shape[0], qkv.shape[1])
    query = (head_norm(qkv[..., :attn].astype(jnp.float32), heads) * scale_q).astype(jnp.bfloat16)
    key = head_norm(qkv[..., attn : 2 * attn].astype(jnp.float32), heads).astype(jnp.bfloat16)
    value = qkv[..., 2 * attn :].reshape(frames, patches, heads, attn // heads)
    scores = jnp.einsum("fphd,gphd->phfg", query, key, preferred_element_type=jnp.float32)
    weights = jnp.exp(scores)
    total = jnp.sum(weights, axis=-1)
    probs = weights.astype(jnp.bfloat16)
    mixed = jnp.einsum("phfg,gphd->fphd", probs, value, preferred_element_type=jnp.float32)
    attended = mixed / jnp.transpose(total, (2, 0, 1))[..., None]
    return attended.astype(jnp.bfloat16).reshape(frames, patches, attn)


def pack_rows(pieces):
    total = sum(p.shape[1] for p in pieces)
    eye = jnp.eye(total, dtype=pieces[0].dtype)
    packed, start = None, 0
    for p in pieces:
        part = jnp.einsum(
            "rc,kc->rk", eye[:, start : start + p.shape[1]], p, preferred_element_type=jnp.float32
        )
        packed = part if packed is None else packed + part
        start += p.shape[1]
    return packed.astype(pieces[0].dtype)


def project(x, gathered):
    count, cols, _ = gathered.shape
    y = jnp.einsum("tk,sck->tsc", x, gathered, preferred_element_type=jnp.float32)
    return y.reshape(x.shape[0], count * cols)


def per_device(
    frames_in,
    modulation,
    self_proj,
    self_out,
    cross_query,
    cross_keyval,
    cross_out,
    text_bank,
    prompt_pick,
    text_lengths,
):
    count = lax.axis_size("seq")
    frame_rows, pixels, width = frames_in.shape
    attn = self_out.shape[0]
    heads = attn // HEAD_DIM
    scale_q = 1.0 / math.sqrt(HEAD_DIM)
    pix_dev = pixels // count
    frames = frame_rows * count
    text_len = text_bank.shape[1]
    txt_dev = text_len // count

    outs_pair = jnp.concatenate([self_out, cross_out], axis=0)
    sizes = (self_proj.shape[1], cross_keyval.shape[1], cross_query.shape[1], outs_pair.shape[1])
    packed = pack_rows([self_proj, cross_keyval, cross_query, outs_pair])
    gathered = lax.all_gather(packed, "seq", axis=0, tiled=False)
    kv_at = sizes[0]
    q_at = kv_at + sizes[1]
    outs_at = q_at + sizes[2]
    query_g = gathered[:, q_at : q_at + sizes[2], :]
    outs_g = gathered[:, outs_at : outs_at + sizes[3], :]

    tokens = frames_in.astype(jnp.float32)
    normed = (layer_norm(tokens) * (1.0 + modulation[1]) + modulation[0]).astype(jnp.bfloat16)
    send = jnp.concatenate(
        [
            normed.reshape(count, pix_dev, width),
            text_bank[0].reshape(count, txt_dev, width),
        ],
        axis=1,
    )
    recv = lax.all_to_all(send, "seq", 0, 0, tiled=True)
    switched = recv[:, :pix_dev, :]
    pick = prompt_pick[0]
    memory_rows = lax.dynamic_index_in_dim(recv[:, pix_dev:, :], pick, 0, keepdims=False)

    flat_pix = switched.reshape(-1, width)
    both = jnp.concatenate([flat_pix, memory_rows], axis=0)
    both_out = jnp.einsum("tk,sck->tsc", both, gathered, preferred_element_type=jnp.float32)
    tok = flat_pix.shape[0]
    qkv = both_out[:tok, :, : sizes[0]].reshape(tok, -1).astype(jnp.bfloat16)
    qkv = qkv.reshape(frames, pix_dev, 3 * attn)
    attended = temporal_attention(qkv, heads, attn, scale_q)

    keyval_rows = both_out[tok:, :, kv_at : kv_at + sizes[1]].reshape(txt_dev, -1).astype(jnp.bfloat16)
    key_rows = head_norm(keyval_rows[:, :attn].astype(jnp.float32), heads).astype(jnp.bfloat16)
    kv_rows = jnp.concatenate([key_rows.reshape(txt_dev, attn), keyval_rows[:, attn:]], axis=1)

    send2 = jnp.concatenate(
        [
            attended.reshape(count, -1),
            jnp.broadcast_to(kv_rows.reshape(1, -1), (count, txt_dev * 2 * attn)),
        ],
        axis=1,
    )
    recv2 = lax.all_to_all(send2, "seq", 0, 0, tiled=True)
    returned = recv2[:, : pix_dev * attn].reshape(pixels, attn)
    keyval = recv2[:, pix_dev * attn :].reshape(text_len, 2 * attn)

    out_self = outs_g[:, :, :attn].reshape(-1, attn)
    out_cross = outs_g[:, :, attn:].reshape(-1, attn)
    self_term = jnp.einsum("ta,ca->tc", returned, out_self, preferred_element_type=jnp.float32)
    after_self = (tokens.reshape(-1, width) + modulation[2] * self_term).astype(jnp.bfloat16)

    text_key = keyval[:, :attn].reshape(text_len, heads, HEAD_DIM)
    text_value = keyval[:, attn:].reshape(text_len, heads, HEAD_DIM)
    slots = jnp.arange(text_lengths.shape[0], dtype=jnp.int32)
    length = jnp.sum(jnp.where(slots == pick, text_lengths, 0))
    live = jnp.arange(text_len, dtype=jnp.int32) < length
    text_query = project(after_self, query_g)
    text_query = (head_norm(text_query, heads) * scale_q).astype(jnp.bfloat16)
    cross_scores = jnp.einsum(
        "thd,lhd->thl", text_query, text_key, preferred_element_type=jnp.float32
    )
    cross_weights = jnp.where(live, jnp.exp(cross_scores), 0.0)
    cross_total = jnp.sum(cross_weights, axis=-1)
    cross_probs = cross_weights.astype(jnp.bfloat16)
    cross_mix = jnp.einsum(
        "thl,lhd->thd", cross_probs, text_value, preferred_element_type=jnp.float32
    )
    crossed = (cross_mix / cross_total[..., None]).astype(jnp.bfloat16).reshape(-1, attn)
    cross_term = jnp.einsum("ta,ca->tc", crossed, out_cross, preferred_element_type=jnp.float32)
    frames_out = (after_self.astype(jnp.float32) + cross_term).astype(jnp.bfloat16)
    return frames_out.reshape(frame_rows, pixels, width)


def solution(mesh):
    placed = (
        P(("clip", "seq"), None, None),
        P("clip", None),
        P(None, "seq"),
        P(None, "seq"),
        P(None, "seq"),
        P(None, "seq"),
        P(None, "seq"),
        P("seq", None, None),
        P("clip"),
        P(),
    )
    return jax.shard_map(
        per_device,
        mesh=mesh,
        in_specs=placed,
        out_specs=P(("clip", "seq"), None, None),
        check_vma=False,
    )
```

```python
import math

import jax
import jax.numpy as jnp
from jax import lax
from jax.sharding import PartitionSpec as P

HEAD_DIM = 72


EPS = 1e-06


def layer_norm(values):
    mean = jnp.mean(values, axis=-1, keepdims=True)
    centred = values - mean
    spread = jnp.mean(centred * centred, axis=-1, keepdims=True)
    return centred * lax.rsqrt(spread + EPS)


def head_norm(values, heads):
    shaped = values.reshape(values.shape[:-1] + (heads, values.shape[-1] // heads))
    power = jnp.mean(shaped * shaped, axis=-1, keepdims=True)
    return shaped * lax.rsqrt(power + EPS)


def temporal_attention(qkv, heads, attn, scale_q):
    frames, patches = (qkv.shape[0], qkv.shape[1])
    query = (head_norm(qkv[..., :attn].astype(jnp.float32), heads) * scale_q).astype(jnp.bfloat16)
    key = head_norm(qkv[..., attn : 2 * attn].astype(jnp.float32), heads).astype(jnp.bfloat16)
    value = qkv[..., 2 * attn :].reshape(frames, patches, heads, attn // heads)
    scores = jnp.einsum("fphd,gphd->phfg", query, key, preferred_element_type=jnp.float32)
    weights = jnp.exp(scores)
    total = jnp.sum(weights, axis=-1)
    probs = weights.astype(jnp.bfloat16)
    mixed = jnp.einsum("phfg,gphd->fphd", probs, value, preferred_element_type=jnp.float32)
    attended = mixed / jnp.transpose(total, (2, 0, 1))[..., None]
    return attended.astype(jnp.bfloat16).reshape(frames, patches, attn)


def pack_rows(pieces):
    total = sum(p.shape[1] for p in pieces)
    eye = jnp.eye(total, dtype=pieces[0].dtype)
    packed, start = None, 0
    for p in pieces:
        part = jnp.einsum(
            "rc,kc->rk", eye[:, start : start + p.shape[1]], p, preferred_element_type=jnp.float32
        )
        packed = part if packed is None else packed + part
        start += p.shape[1]
    return packed.astype(pieces[0].dtype)


def project(x, gathered):
    count, cols, _ = gathered.shape
    y = jnp.einsum("tk,sck->tsc", x, gathered, preferred_element_type=jnp.float32)
    return y.reshape(x.shape[0], count * cols)


def per_device(
    frames_in,
    modulation,
    self_proj,
    self_out,
    cross_query,
    cross_keyval,
    cross_out,
    text_bank,
    prompt_pick,
    text_lengths,
):
    count = lax.axis_size("seq")
    frame_rows, pixels, width = frames_in.shape
    attn = self_out.shape[0]
    heads = attn // HEAD_DIM
    scale_q = 1.0 / math.sqrt(HEAD_DIM)
    pix_dev = pixels // count
    frames = frame_rows * count
    text_len = text_bank.shape[1]
    txt_dev = text_len // count

    outs_pair = jnp.concatenate([self_out, cross_out], axis=0)
    sizes = (self_proj.shape[1], cross_keyval.shape[1], cross_query.shape[1])
    pad = -sum(sizes) % 16
    packed = pack_rows([self_proj, cross_keyval, cross_query, jnp.zeros((width, pad), self_proj.dtype)])
    gathered = lax.all_gather(packed, "seq", axis=0, tiled=False)
    kv_at = sizes[0]
    q_at = kv_at + sizes[1]
    query_g = gathered[:, q_at : q_at + sizes[2], :]
    outs_t = pack_rows([outs_pair])

    tokens = frames_in.astype(jnp.float32)
    normed = (layer_norm(tokens) * (1.0 + modulation[1]) + modulation[0]).astype(jnp.bfloat16)
    send = jnp.concatenate(
        [
            normed.reshape(count, pix_dev, width),
            text_bank[0].reshape(count, txt_dev, width),
            jnp.broadcast_to(outs_t[None], (count,) + outs_t.shape),
        ],
        axis=1,
    )
    recv = lax.all_to_all(send, "seq", 0, 0, tiled=True)
    switched = recv[:, :pix_dev, :]
    pick = prompt_pick[0]
    memory_rows = lax.dynamic_index_in_dim(recv[:, pix_dev : pix_dev + txt_dev, :], pick, 0, keepdims=False)
    outs_g = recv[:, pix_dev + txt_dev :, :]

    flat_pix = switched.reshape(-1, width)
    both = jnp.concatenate([flat_pix, memory_rows], axis=0)
    both_out = jnp.einsum("tk,sck->tsc", both, gathered, preferred_element_type=jnp.float32)
    tok = flat_pix.shape[0]
    qkv = both_out[:tok, :, : sizes[0]].reshape(tok, -1).astype(jnp.bfloat16)
    qkv = qkv.reshape(frames, pix_dev, 3 * attn)
    attended = temporal_attention(qkv, heads, attn, scale_q)

    keyval_rows = both_out[tok:, :, kv_at : kv_at + sizes[1]].reshape(txt_dev, -1).astype(jnp.bfloat16)
    key_rows = head_norm(keyval_rows[:, :attn].astype(jnp.float32), heads).astype(jnp.bfloat16)
    kv_rows = jnp.concatenate([key_rows.reshape(txt_dev, attn), keyval_rows[:, attn:]], axis=1)

    send2 = jnp.concatenate(
        [
            attended.reshape(count, -1),
            jnp.broadcast_to(kv_rows.reshape(1, -1), (count, txt_dev * 2 * attn)),
        ],
        axis=1,
    )
    recv2 = lax.all_to_all(send2, "seq", 0, 0, tiled=True)
    returned = recv2[:, : pix_dev * attn].reshape(pixels, attn)
    keyval = recv2[:, pix_dev * attn :].reshape(text_len, 2 * attn)

    out_self = outs_g[:, :, :attn].reshape(-1, attn)
    out_cross = outs_g[:, :, attn:].reshape(-1, attn)
    self_term = jnp.einsum("ta,ca->tc", returned, out_self, preferred_element_type=jnp.float32)
    after_self = (tokens.reshape(-1, width) + modulation[2] * self_term).astype(jnp.bfloat16)

    text_key = keyval[:, :attn].reshape(text_len, heads, HEAD_DIM)
    text_value = keyval[:, attn:].reshape(text_len, heads, HEAD_DIM)
    slots = jnp.arange(text_lengths.shape[0], dtype=jnp.int32)
    length = jnp.sum(jnp.where(slots == pick, text_lengths, 0))
    live = jnp.arange(text_len, dtype=jnp.int32) < length
    text_query = project(after_self, query_g)
    text_query = (head_norm(text_query, heads) * scale_q).astype(jnp.bfloat16)
    cross_scores = jnp.einsum(
        "thd,lhd->thl", text_query, text_key, preferred_element_type=jnp.float32
    )
    cross_weights = jnp.where(live, jnp.exp(cross_scores), 0.0)
    cross_total = jnp.sum(cross_weights, axis=-1)
    cross_probs = cross_weights.astype(jnp.bfloat16)
    cross_mix = jnp.einsum(
        "thl,lhd->thd", cross_probs, text_value, preferred_element_type=jnp.float32
    )
    crossed = (cross_mix / cross_total[..., None]).astype(jnp.bfloat16).reshape(-1, attn)
    cross_term = jnp.einsum("ta,ca->tc", crossed, out_cross, preferred_element_type=jnp.float32)
    frames_out = (after_self.astype(jnp.float32) + cross_term).astype(jnp.bfloat16)
    return frames_out.reshape(frame_rows, pixels, width)


def solution(mesh):
    placed = (
        P(("clip", "seq"), None, None),
        P("clip", None),
        P(None, "seq"),
        P(None, "seq"),
        P(None, "seq"),
        P(None, "seq"),
        P(None, "seq"),
        P("seq", None, None),
        P("clip"),
        P(),
    )
    return jax.shard_map(
        per_device,
        mesh=mesh,
        in_specs=placed,
        out_specs=P(("clip", "seq"), None, None),
        check_vma=False,
    )
```

```python
import math

import jax
import jax.numpy as jnp
from jax import lax
from jax.sharding import PartitionSpec as P

HEAD_DIM = 72


EPS = 1e-06


def layer_norm(values):
    mean = jnp.mean(values, axis=-1, keepdims=True)
    centred = values - mean
    spread = jnp.mean(centred * centred, axis=-1, keepdims=True)
    return centred * lax.rsqrt(spread + EPS)


def head_norm(values, heads):
    shaped = values.reshape(values.shape[:-1] + (heads, values.shape[-1] // heads))
    power = jnp.mean(shaped * shaped, axis=-1, keepdims=True)
    return shaped * lax.rsqrt(power + EPS)


def temporal_attention(qkv, heads, attn, scale_q):
    frames, patches = (qkv.shape[0], qkv.shape[1])
    query = (head_norm(qkv[..., :attn].astype(jnp.float32), heads) * scale_q).astype(jnp.bfloat16)
    key = head_norm(qkv[..., attn : 2 * attn].astype(jnp.float32), heads).astype(jnp.bfloat16)
    value = qkv[..., 2 * attn :].reshape(frames, patches, heads, attn // heads)
    scores = jnp.einsum("fphd,gphd->phfg", query, key, preferred_element_type=jnp.float32)
    weights = jnp.exp(scores)
    total = jnp.sum(weights, axis=-1)
    probs = weights.astype(jnp.bfloat16)
    mixed = jnp.einsum("phfg,gphd->fphd", probs, value, preferred_element_type=jnp.float32)
    attended = mixed / jnp.transpose(total, (2, 0, 1))[..., None]
    return attended.astype(jnp.bfloat16).reshape(frames, patches, attn)


def pack_rows(pieces):
    total = sum(p.shape[1] for p in pieces)
    eye = jnp.eye(total, dtype=pieces[0].dtype)
    packed, start = None, 0
    for p in pieces:
        part = jnp.einsum(
            "rc,kc->rk", eye[:, start : start + p.shape[1]], p, preferred_element_type=jnp.float32
        )
        packed = part if packed is None else packed + part
        start += p.shape[1]
    return packed.astype(pieces[0].dtype)


def project(x, gathered):
    count, cols, _ = gathered.shape
    y = jnp.einsum("tk,sck->tsc", x, gathered, preferred_element_type=jnp.float32)
    return y.reshape(x.shape[0], count * cols)


def per_device(
    frames_in,
    modulation,
    self_proj,
    self_out,
    cross_query,
    cross_keyval,
    cross_out,
    text_bank,
    prompt_pick,
    text_lengths,
):
    count = lax.axis_size("seq")
    frame_rows, pixels, width = frames_in.shape
    attn = self_out.shape[0]
    heads = attn // HEAD_DIM
    scale_q = 1.0 / math.sqrt(HEAD_DIM)
    pix_dev = pixels // count
    frames = frame_rows * count
    text_len = text_bank.shape[1]
    txt_dev = text_len // count

    outs_pair = jnp.concatenate([self_out, cross_out], axis=0)
    sizes = (self_proj.shape[1], cross_query.shape[1], outs_pair.shape[1])
    pad = -sum(sizes) % 16
    packed = pack_rows([self_proj, cross_query, outs_pair, jnp.zeros((width, pad), self_proj.dtype)])
    gathered = lax.all_gather(packed, "seq", axis=0, tiled=False)
    q_at = sizes[0]
    outs_at = q_at + sizes[1]
    query_g = gathered[:, q_at : q_at + sizes[1], :]
    outs_g = gathered[:, outs_at : outs_at + sizes[2], :]

    tokens = frames_in.astype(jnp.float32)
    normed = (layer_norm(tokens) * (1.0 + modulation[1]) + modulation[0]).astype(jnp.bfloat16)
    send = jnp.concatenate(
        [
            normed.reshape(count, pix_dev, width),
            text_bank[0].reshape(count, txt_dev, width),
        ],
        axis=1,
    )
    recv = lax.all_to_all(send, "seq", 0, 0, tiled=True)
    switched = recv[:, :pix_dev, :]
    pick = prompt_pick[0]
    memory_rows = lax.dynamic_index_in_dim(recv[:, pix_dev:, :], pick, 0, keepdims=False)

    spread = jnp.broadcast_to(memory_rows[None], (count,) + memory_rows.shape)
    memory = lax.all_to_all(spread, "seq", 0, 0, tiled=True).reshape(text_len, width)
    kv_cols = jnp.dot(memory, cross_keyval, preferred_element_type=jnp.float32).astype(jnp.bfloat16)

    flat_pix = switched.reshape(-1, width)
    qkv_all = jnp.einsum("tk,sck->tsc", flat_pix, gathered, preferred_element_type=jnp.float32)
    qkv = qkv_all[:, :, : sizes[0]].reshape(flat_pix.shape[0], -1).astype(jnp.bfloat16)
    qkv = qkv.reshape(frames, pix_dev, 3 * attn)
    attended = temporal_attention(qkv, heads, attn, scale_q)

    send2 = jnp.concatenate(
        [
            attended.reshape(count, -1),
            jnp.broadcast_to(kv_cols.reshape(1, -1), (count, kv_cols.size)),
        ],
        axis=1,
    )
    recv2 = lax.all_to_all(send2, "seq", 0, 0, tiled=True)
    returned = recv2[:, : pix_dev * attn].reshape(pixels, attn)
    keyval = recv2[:, pix_dev * attn :].reshape(count, text_len, -1).transpose(1, 0, 2).reshape(text_len, 2 * attn)

    out_self = outs_g[:, :, :attn].reshape(-1, attn)
    out_cross = outs_g[:, :, attn:].reshape(-1, attn)
    self_term = jnp.einsum("ta,ca->tc", returned, out_self, preferred_element_type=jnp.float32)
    after_self = (tokens.reshape(-1, width) + modulation[2] * self_term).astype(jnp.bfloat16)

    text_key = head_norm(keyval[:, :attn].astype(jnp.float32), heads).astype(jnp.bfloat16)
    text_value = keyval[:, attn:].reshape(text_len, heads, HEAD_DIM)
    slots = jnp.arange(text_lengths.shape[0], dtype=jnp.int32)
    length = jnp.sum(jnp.where(slots == pick, text_lengths, 0))
    live = jnp.arange(text_len, dtype=jnp.int32) < length
    text_query = project(after_self, query_g)
    text_query = (head_norm(text_query, heads) * scale_q).astype(jnp.bfloat16)
    cross_scores = jnp.einsum(
        "thd,lhd->thl", text_query, text_key, preferred_element_type=jnp.float32
    )
    cross_weights = jnp.where(live, jnp.exp(cross_scores), 0.0)
    cross_total = jnp.sum(cross_weights, axis=-1)
    cross_probs = cross_weights.astype(jnp.bfloat16)
    cross_mix = jnp.einsum(
        "thl,lhd->thd", cross_probs, text_value, preferred_element_type=jnp.float32
    )
    crossed = (cross_mix / cross_total[..., None]).astype(jnp.bfloat16).reshape(-1, attn)
    cross_term = jnp.einsum("ta,ca->tc", crossed, out_cross, preferred_element_type=jnp.float32)
    frames_out = (after_self.astype(jnp.float32) + cross_term).astype(jnp.bfloat16)
    return frames_out.reshape(frame_rows, pixels, width)


def solution(mesh):
    placed = (
        P(("clip", "seq"), None, None),
        P("clip", None),
        P(None, "seq"),
        P(None, "seq"),
        P(None, "seq"),
        P(None, "seq"),
        P(None, "seq"),
        P("seq", None, None),
        P("clip"),
        P(),
    )
    return jax.shard_map(
        per_device,
        mesh=mesh,
        in_specs=placed,
        out_specs=P(("clip", "seq"), None, None),
        check_vma=False,
    )
```

```python
import math

import jax
import jax.numpy as jnp
from jax import lax
from jax.sharding import PartitionSpec as P

HEAD_DIM = 72


EPS = 1e-06


def layer_norm(values):
    mean = jnp.mean(values, axis=-1, keepdims=True)
    centred = values - mean
    spread = jnp.mean(centred * centred, axis=-1, keepdims=True)
    return centred * lax.rsqrt(spread + EPS)


def head_norm(values, heads):
    shaped = values.reshape(values.shape[:-1] + (heads, values.shape[-1] // heads))
    power = jnp.mean(shaped * shaped, axis=-1, keepdims=True)
    return shaped * lax.rsqrt(power + EPS)


def temporal_attention(qkv, heads, attn, scale_q, patches):
    tokens = qkv.shape[0]
    query = (head_norm(qkv[:, :attn].astype(jnp.float32), heads) * scale_q).astype(jnp.bfloat16)
    key = head_norm(qkv[:, attn : 2 * attn].astype(jnp.float32), heads).astype(jnp.bfloat16)
    value = qkv[:, 2 * attn :].reshape(tokens, heads, attn // heads)
    scores = jnp.einsum("thd,uhd->htu", query, key, preferred_element_type=jnp.float32)
    patch = jnp.arange(tokens, dtype=jnp.int32) % patches
    same = patch[:, None] == patch[None, :]
    weights = jnp.where(same, jnp.exp(scores), 0.0)
    total = jnp.sum(weights, axis=-1)
    probs = weights.astype(jnp.bfloat16)
    mixed = jnp.einsum("htu,uhd->thd", probs, value, preferred_element_type=jnp.float32)
    attended = mixed / jnp.transpose(total)[..., None]
    return attended.astype(jnp.bfloat16).reshape(tokens, attn)


def pack_rows(pieces):
    total = sum(p.shape[1] for p in pieces)
    eye = jnp.eye(total, dtype=pieces[0].dtype)
    packed, start = None, 0
    for p in pieces:
        part = jnp.einsum(
            "rc,kc->rk", eye[:, start : start + p.shape[1]], p, preferred_element_type=jnp.float32
        )
        packed = part if packed is None else packed + part
        start += p.shape[1]
    return packed.astype(pieces[0].dtype)


def project(x, gathered):
    count, cols, _ = gathered.shape
    y = jnp.einsum("tk,sck->tsc", x, gathered, preferred_element_type=jnp.float32)
    return y.reshape(x.shape[0], count * cols)


def per_device(
    frames_in,
    modulation,
    self_proj,
    self_out,
    cross_query,
    cross_keyval,
    cross_out,
    text_bank,
    prompt_pick,
    text_lengths,
):
    count = lax.axis_size("seq")
    frame_rows, pixels, width = frames_in.shape
    attn = self_out.shape[0]
    heads = attn // HEAD_DIM
    scale_q = 1.0 / math.sqrt(HEAD_DIM)
    pix_dev = pixels // count
    frames = frame_rows * count
    text_len = text_bank.shape[1]
    txt_dev = text_len // count

    outs_pair = jnp.concatenate([self_out, cross_out], axis=0)
    sizes = (self_proj.shape[1], cross_keyval.shape[1], cross_query.shape[1], outs_pair.shape[1])
    packed = pack_rows([self_proj, cross_keyval, cross_query, outs_pair])
    gathered = lax.all_gather(packed, "seq", axis=0, tiled=False)
    kv_at = sizes[0]
    q_at = kv_at + sizes[1]
    outs_at = q_at + sizes[2]
    query_g = gathered[:, q_at : q_at + sizes[2], :]
    outs_g = gathered[:, outs_at : outs_at + sizes[3], :]

    tokens = frames_in.astype(jnp.float32)
    normed = (layer_norm(tokens) * (1.0 + modulation[1]) + modulation[0]).astype(jnp.bfloat16)
    send = jnp.concatenate(
        [
            normed.reshape(count, pix_dev, width),
            text_bank[0].reshape(count, txt_dev, width),
        ],
        axis=1,
    )
    recv = lax.all_to_all(send, "seq", 0, 0, tiled=True)
    switched = recv[:, :pix_dev, :]
    pick = prompt_pick[0]
    memory_rows = lax.dynamic_index_in_dim(recv[:, pix_dev:, :], pick, 0, keepdims=False)

    flat_pix = switched.reshape(-1, width)
    both = jnp.concatenate([flat_pix, memory_rows], axis=0)
    both_out = jnp.einsum("tk,sck->tsc", both, gathered, preferred_element_type=jnp.float32)
    tok = flat_pix.shape[0]
    qkv = both_out[:tok, :, : sizes[0]].reshape(tok, -1).astype(jnp.bfloat16)
    attended = temporal_attention(qkv, heads, attn, scale_q, pix_dev)

    keyval_rows = both_out[tok:, :, kv_at : kv_at + sizes[1]].reshape(txt_dev, -1).astype(jnp.bfloat16)
    key_rows = head_norm(keyval_rows[:, :attn].astype(jnp.float32), heads).astype(jnp.bfloat16)
    kv_rows = jnp.concatenate([key_rows.reshape(txt_dev, attn), keyval_rows[:, attn:]], axis=1)

    send2 = jnp.concatenate(
        [
            attended.reshape(count, -1),
            jnp.broadcast_to(kv_rows.reshape(1, -1), (count, txt_dev * 2 * attn)),
        ],
        axis=1,
    )
    recv2 = lax.all_to_all(send2, "seq", 0, 0, tiled=True)
    returned = recv2[:, : pix_dev * attn].reshape(pixels, attn)
    keyval = recv2[:, pix_dev * attn :].reshape(text_len, 2 * attn)

    out_self = outs_g[:, :, :attn].reshape(-1, attn)
    out_cross = outs_g[:, :, attn:].reshape(-1, attn)
    self_term = jnp.einsum("ta,ca->tc", returned, out_self, preferred_element_type=jnp.float32)
    after_self = (tokens.reshape(-1, width) + modulation[2] * self_term).astype(jnp.bfloat16)

    text_key = keyval[:, :attn].reshape(text_len, heads, HEAD_DIM)
    text_value = keyval[:, attn:].reshape(text_len, heads, HEAD_DIM)
    slots = jnp.arange(text_lengths.shape[0], dtype=jnp.int32)
    length = jnp.sum(jnp.where(slots == pick, text_lengths, 0))
    live = jnp.arange(text_len, dtype=jnp.int32) < length
    text_query = project(after_self, query_g)
    text_query = (head_norm(text_query, heads) * scale_q).astype(jnp.bfloat16)
    cross_scores = jnp.einsum(
        "thd,lhd->thl", text_query, text_key, preferred_element_type=jnp.float32
    )
    cross_weights = jnp.where(live, jnp.exp(cross_scores), 0.0)
    cross_total = jnp.sum(cross_weights, axis=-1)
    cross_probs = cross_weights.astype(jnp.bfloat16)
    cross_mix = jnp.einsum(
        "thl,lhd->thd", cross_probs, text_value, preferred_element_type=jnp.float32
    )
    crossed = (cross_mix / cross_total[..., None]).astype(jnp.bfloat16).reshape(-1, attn)
    cross_term = jnp.einsum("ta,ca->tc", crossed, out_cross, preferred_element_type=jnp.float32)
    frames_out = (after_self.astype(jnp.float32) + cross_term).astype(jnp.bfloat16)
    return frames_out.reshape(frame_rows, pixels, width)


def solution(mesh):
    placed = (
        P(("clip", "seq"), None, None),
        P("clip", None),
        P(None, "seq"),
        P(None, "seq"),
        P(None, "seq"),
        P(None, "seq"),
        P(None, "seq"),
        P("seq", None, None),
        P("clip"),
        P(),
    )
    return jax.shard_map(
        per_device,
        mesh=mesh,
        in_specs=placed,
        out_specs=P(("clip", "seq"), None, None),
        check_vma=False,
    )
```

```python
import math

import jax
import jax.numpy as jnp
from jax import lax
from jax.sharding import PartitionSpec as P

HEAD_DIM = 72


EPS = 1e-06


def layer_norm(values):
    mean = jnp.mean(values, axis=-1, keepdims=True)
    centred = values - mean
    spread = jnp.mean(centred * centred, axis=-1, keepdims=True)
    return centred * lax.rsqrt(spread + EPS)


def head_norm(values, heads):
    shaped = values.reshape(values.shape[:-1] + (heads, values.shape[-1] // heads))
    power = jnp.mean(shaped * shaped, axis=-1, keepdims=True)
    return shaped * lax.rsqrt(power + EPS)


def temporal_attention(qkv, heads, attn, scale_q, patches):
    tokens = qkv.shape[0]
    query = (head_norm(qkv[:, :attn].astype(jnp.float32), heads) * scale_q).astype(jnp.bfloat16)
    key = head_norm(qkv[:, attn : 2 * attn].astype(jnp.float32), heads).astype(jnp.bfloat16)
    value = qkv[:, 2 * attn :].reshape(tokens, heads, attn // heads)
    scores = jnp.einsum("thd,uhd->htu", query, key, preferred_element_type=jnp.float32)
    patch = jnp.arange(tokens, dtype=jnp.int32) % patches
    same = patch[:, None] == patch[None, :]
    weights = jnp.where(same, jnp.exp(scores), 0.0)
    total = jnp.sum(weights, axis=-1)
    probs = weights.astype(jnp.bfloat16)
    mixed = jnp.einsum("htu,uhd->thd", probs, value, preferred_element_type=jnp.float32)
    attended = mixed / jnp.transpose(total)[..., None]
    return attended.astype(jnp.bfloat16).reshape(tokens, attn)


def pack_rows(pieces):
    total = sum(p.shape[1] for p in pieces)
    eye = jnp.eye(total, dtype=pieces[0].dtype)
    packed, start = None, 0
    for p in pieces:
        part = jnp.einsum(
            "rc,kc->rk", eye[:, start : start + p.shape[1]], p, preferred_element_type=jnp.float32
        )
        packed = part if packed is None else packed + part
        start += p.shape[1]
    return packed.astype(pieces[0].dtype)


def project(x, gathered):
    count, cols, _ = gathered.shape
    y = jnp.einsum("tk,sck->tsc", x, gathered, preferred_element_type=jnp.float32)
    return y.reshape(x.shape[0], count * cols)


def per_device(
    frames_in,
    modulation,
    self_proj,
    self_out,
    cross_query,
    cross_keyval,
    cross_out,
    text_bank,
    prompt_pick,
    text_lengths,
):
    count = lax.axis_size("seq")
    frame_rows, pixels, width = frames_in.shape
    attn = self_out.shape[0]
    heads = attn // HEAD_DIM
    scale_q = 1.0 / math.sqrt(HEAD_DIM)
    pix_dev = pixels // count
    frames = frame_rows * count
    text_len = text_bank.shape[1]
    txt_dev = text_len // count

    outs_pair = jnp.concatenate([self_out, cross_out], axis=0)
    sizes = (self_proj.shape[1], cross_keyval.shape[1], cross_query.shape[1], outs_pair.shape[1])
    packed = pack_rows([self_proj, cross_keyval, cross_query, outs_pair])
    gathered = lax.all_gather(packed, "seq", axis=0, tiled=False)
    kv_at = sizes[0]
    q_at = kv_at + sizes[1]
    outs_at = q_at + sizes[2]
    query_g = gathered[:, q_at : q_at + sizes[2], :]
    outs_g = gathered[:, outs_at : outs_at + sizes[3], :]

    tokens = frames_in.astype(jnp.float32)
    normed = (layer_norm(tokens) * (1.0 + modulation[1]) + modulation[0]).astype(jnp.bfloat16)
    send = jnp.concatenate(
        [
            normed.reshape(count, pix_dev, width),
            text_bank[0].reshape(count, txt_dev, width),
        ],
        axis=1,
    )
    recv = lax.all_to_all(send, "seq", 0, 0, tiled=True)
    switched = recv[:, :pix_dev, :]
    pick = prompt_pick[0]
    memory_rows = lax.dynamic_index_in_dim(recv[:, pix_dev:, :], pick, 0, keepdims=False)

    flat_pix = switched.reshape(-1, width)
    both = jnp.concatenate([flat_pix, memory_rows], axis=0)
    lead = -(-(kv_at + sizes[1]) // 16) * 16
    both_out = jnp.einsum(
        "tk,sck->tsc", both, gathered[:, :lead, :], preferred_element_type=jnp.float32
    )
    tok = flat_pix.shape[0]
    qkv = both_out[:tok, :, : sizes[0]].reshape(tok, -1).astype(jnp.bfloat16)
    attended = temporal_attention(qkv, heads, attn, scale_q, pix_dev)

    keyval_rows = both_out[tok:, :, kv_at : kv_at + sizes[1]].reshape(txt_dev, -1).astype(jnp.bfloat16)
    key_rows = head_norm(keyval_rows[:, :attn].astype(jnp.float32), heads).astype(jnp.bfloat16)
    kv_rows = jnp.concatenate([key_rows.reshape(txt_dev, attn), keyval_rows[:, attn:]], axis=1)

    send2 = jnp.concatenate(
        [
            attended.reshape(count, -1),
            jnp.broadcast_to(kv_rows.reshape(1, -1), (count, txt_dev * 2 * attn)),
        ],
        axis=1,
    )
    recv2 = lax.all_to_all(send2, "seq", 0, 0, tiled=True)
    returned = recv2[:, : pix_dev * attn].reshape(pixels, attn)
    keyval = recv2[:, pix_dev * attn :].reshape(text_len, 2 * attn)

    out_self = outs_g[:, :, :attn].reshape(-1, attn)
    out_cross = outs_g[:, :, attn:].reshape(-1, attn)
    self_term = jnp.einsum("ta,ca->tc", returned, out_self, preferred_element_type=jnp.float32)
    after_self = (tokens.reshape(-1, width) + modulation[2] * self_term).astype(jnp.bfloat16)

    text_key = keyval[:, :attn].reshape(text_len, heads, HEAD_DIM)
    text_value = keyval[:, attn:].reshape(text_len, heads, HEAD_DIM)
    slots = jnp.arange(text_lengths.shape[0], dtype=jnp.int32)
    length = jnp.sum(jnp.where(slots == pick, text_lengths, 0))
    live = jnp.arange(text_len, dtype=jnp.int32) < length
    text_query = project(after_self, query_g)
    text_query = (head_norm(text_query, heads) * scale_q).astype(jnp.bfloat16)
    cross_scores = jnp.einsum(
        "thd,lhd->thl", text_query, text_key, preferred_element_type=jnp.float32
    )
    cross_weights = jnp.where(live, jnp.exp(cross_scores), 0.0)
    cross_total = jnp.sum(cross_weights, axis=-1)
    cross_probs = cross_weights.astype(jnp.bfloat16)
    cross_mix = jnp.einsum(
        "thl,lhd->thd", cross_probs, text_value, preferred_element_type=jnp.float32
    )
    crossed = (cross_mix / cross_total[..., None]).astype(jnp.bfloat16).reshape(-1, attn)
    cross_term = jnp.einsum("ta,ca->tc", crossed, out_cross, preferred_element_type=jnp.float32)
    frames_out = (after_self.astype(jnp.float32) + cross_term).astype(jnp.bfloat16)
    return frames_out.reshape(frame_rows, pixels, width)


def solution(mesh):
    placed = (
        P(("clip", "seq"), None, None),
        P("clip", None),
        P(None, "seq"),
        P(None, "seq"),
        P(None, "seq"),
        P(None, "seq"),
        P(None, "seq"),
        P("seq", None, None),
        P("clip"),
        P(),
    )
    return jax.shard_map(
        per_device,
        mesh=mesh,
        in_specs=placed,
        out_specs=P(("clip", "seq"), None, None),
        check_vma=False,
    )
```

```python
import math

import jax
import jax.numpy as jnp
from jax import lax
from jax.sharding import PartitionSpec as P

HEAD_DIM = 72


EPS = 1e-06


def layer_norm(values):
    mean = jnp.mean(values, axis=-1, keepdims=True)
    centred = values - mean
    spread = jnp.mean(centred * centred, axis=-1, keepdims=True)
    return centred * lax.rsqrt(spread + EPS)


def head_norm(values, heads):
    shaped = values.reshape(values.shape[:-1] + (heads, values.shape[-1] // heads))
    power = jnp.mean(shaped * shaped, axis=-1, keepdims=True)
    return shaped * lax.rsqrt(power + EPS)


def temporal_attention(qkv, heads, attn, scale_q, patches):
    tokens = qkv.shape[0]
    query = (head_norm(qkv[:, :attn].astype(jnp.float32), heads) * scale_q).astype(jnp.bfloat16)
    key = head_norm(qkv[:, attn : 2 * attn].astype(jnp.float32), heads).astype(jnp.bfloat16)
    value = qkv[:, 2 * attn :].reshape(tokens, heads, attn // heads)
    scores = jnp.einsum("thd,uhd->htu", query, key, preferred_element_type=jnp.float32)
    patch = jnp.arange(tokens, dtype=jnp.int32) % patches
    same = patch[:, None] == patch[None, :]
    weights = jnp.where(same, jnp.exp(scores), 0.0)
    total = jnp.sum(weights, axis=-1)
    probs = weights.astype(jnp.bfloat16)
    mixed = jnp.einsum("htu,uhd->thd", probs, value, preferred_element_type=jnp.float32)
    attended = mixed / jnp.transpose(total)[..., None]
    return attended.astype(jnp.bfloat16).reshape(tokens, attn)


def pack_rows(pieces):
    joined = jnp.concatenate(pieces, axis=1)
    eye = jnp.eye(joined.shape[1], dtype=joined.dtype)
    return jnp.einsum("rc,kc->rk", eye, joined, preferred_element_type=joined.dtype)


def project(x, gathered):
    count, cols, _ = gathered.shape
    y = jnp.einsum("tk,sck->tsc", x, gathered, preferred_element_type=jnp.float32)
    return y.reshape(x.shape[0], count * cols)


def per_device(
    frames_in,
    modulation,
    self_proj,
    self_out,
    cross_query,
    cross_keyval,
    cross_out,
    text_bank,
    prompt_pick,
    text_lengths,
):
    count = lax.axis_size("seq")
    frame_rows, pixels, width = frames_in.shape
    attn = self_out.shape[0]
    heads = attn // HEAD_DIM
    scale_q = 1.0 / math.sqrt(HEAD_DIM)
    pix_dev = pixels // count
    frames = frame_rows * count
    text_len = text_bank.shape[1]
    txt_dev = text_len // count

    outs_pair = jnp.concatenate([self_out, cross_out], axis=0)
    sizes = (self_proj.shape[1], cross_keyval.shape[1], cross_query.shape[1], outs_pair.shape[1])
    packed = pack_rows([self_proj, cross_keyval, cross_query, outs_pair])
    gathered = lax.all_gather(packed, "seq", axis=0, tiled=False)
    kv_at = sizes[0]
    q_at = kv_at + sizes[1]
    outs_at = q_at + sizes[2]
    query_g = gathered[:, q_at : q_at + sizes[2], :]
    outs_g = gathered[:, outs_at : outs_at + sizes[3], :]

    tokens = frames_in.astype(jnp.float32)
    normed = (layer_norm(tokens) * (1.0 + modulation[1]) + modulation[0]).astype(jnp.bfloat16)
    send = jnp.concatenate(
        [
            normed.reshape(count, pix_dev, width),
            text_bank[0].reshape(count, txt_dev, width),
        ],
        axis=1,
    )
    recv = lax.all_to_all(send, "seq", 0, 0, tiled=True)
    switched = recv[:, :pix_dev, :]
    pick = prompt_pick[0]
    memory_rows = lax.dynamic_index_in_dim(recv[:, pix_dev:, :], pick, 0, keepdims=False)

    flat_pix = switched.reshape(-1, width)
    both = jnp.concatenate([flat_pix, memory_rows], axis=0)
    lead = -(-(kv_at + sizes[1]) // 16) * 16
    both_out = jnp.einsum(
        "tk,sck->tsc", both, gathered[:, :lead, :], preferred_element_type=jnp.float32
    )
    tok = flat_pix.shape[0]
    qkv = both_out[:tok, :, : sizes[0]].reshape(tok, -1).astype(jnp.bfloat16)
    attended = temporal_attention(qkv, heads, attn, scale_q, pix_dev)

    keyval_rows = both_out[tok:, :, kv_at : kv_at + sizes[1]].reshape(txt_dev, -1).astype(jnp.bfloat16)
    key_rows = head_norm(keyval_rows[:, :attn].astype(jnp.float32), heads).astype(jnp.bfloat16)
    kv_rows = jnp.concatenate([key_rows.reshape(txt_dev, attn), keyval_rows[:, attn:]], axis=1)

    send2 = jnp.concatenate(
        [
            attended.reshape(count, -1),
            jnp.broadcast_to(kv_rows.reshape(1, -1), (count, txt_dev * 2 * attn)),
        ],
        axis=1,
    )
    recv2 = lax.all_to_all(send2, "seq", 0, 0, tiled=True)
    returned = recv2[:, : pix_dev * attn].reshape(pixels, attn)
    keyval = recv2[:, pix_dev * attn :].reshape(text_len, 2 * attn)

    out_self = outs_g[:, :, :attn].reshape(-1, attn)
    out_cross = outs_g[:, :, attn:].reshape(-1, attn)
    self_term = jnp.einsum("ta,ca->tc", returned, out_self, preferred_element_type=jnp.float32)
    after_self = (tokens.reshape(-1, width) + modulation[2] * self_term).astype(jnp.bfloat16)

    text_key = keyval[:, :attn].reshape(text_len, heads, HEAD_DIM)
    text_value = keyval[:, attn:].reshape(text_len, heads, HEAD_DIM)
    slots = jnp.arange(text_lengths.shape[0], dtype=jnp.int32)
    length = jnp.sum(jnp.where(slots == pick, text_lengths, 0))
    live = jnp.arange(text_len, dtype=jnp.int32) < length
    text_query = project(after_self, query_g)
    text_query = (head_norm(text_query, heads) * scale_q).astype(jnp.bfloat16)
    cross_scores = jnp.einsum(
        "thd,lhd->thl", text_query, text_key, preferred_element_type=jnp.float32
    )
    cross_weights = jnp.where(live, jnp.exp(cross_scores), 0.0)
    cross_total = jnp.sum(cross_weights, axis=-1)
    cross_probs = cross_weights.astype(jnp.bfloat16)
    cross_mix = jnp.einsum(
        "thl,lhd->thd", cross_probs, text_value, preferred_element_type=jnp.float32
    )
    crossed = (cross_mix / cross_total[..., None]).astype(jnp.bfloat16).reshape(-1, attn)
    cross_term = jnp.einsum("ta,ca->tc", crossed, out_cross, preferred_element_type=jnp.float32)
    frames_out = (after_self.astype(jnp.float32) + cross_term).astype(jnp.bfloat16)
    return frames_out.reshape(frame_rows, pixels, width)


def solution(mesh):
    placed = (
        P(("clip", "seq"), None, None),
        P("clip", None),
        P(None, "seq"),
        P(None, "seq"),
        P(None, "seq"),
        P(None, "seq"),
        P(None, "seq"),
        P("seq", None, None),
        P("clip"),
        P(),
    )
    return jax.shard_map(
        per_device,
        mesh=mesh,
        in_specs=placed,
        out_specs=P(("clip", "seq"), None, None),
        check_vma=False,
    )
```

```python
import math

import jax
import jax.numpy as jnp
from jax import lax
from jax.sharding import PartitionSpec as P

HEAD_DIM = 72


EPS = 1e-06


def layer_norm(values):
    mean = jnp.mean(values, axis=-1, keepdims=True)
    centred = values - mean
    spread = jnp.mean(centred * centred, axis=-1, keepdims=True)
    return centred * lax.rsqrt(spread + EPS)


def head_norm(values, heads):
    shaped = values.reshape(values.shape[:-1] + (heads, values.shape[-1] // heads))
    power = jnp.mean(shaped * shaped, axis=-1, keepdims=True)
    return shaped * lax.rsqrt(power + EPS)


def temporal_attention(qkv, heads, attn, scale_q, patches):
    tokens = qkv.shape[0]
    query = (head_norm(qkv[:, :attn].astype(jnp.float32), heads) * scale_q).astype(jnp.bfloat16)
    key = head_norm(qkv[:, attn : 2 * attn].astype(jnp.float32), heads).astype(jnp.bfloat16)
    value = qkv[:, 2 * attn :].reshape(tokens, heads, attn // heads)
    scores = jnp.einsum("thd,uhd->htu", query, key, preferred_element_type=jnp.float32)
    patch = jnp.arange(tokens, dtype=jnp.int32) % patches
    same = patch[:, None] == patch[None, :]
    weights = jnp.where(same, jnp.exp(scores), 0.0)
    total = jnp.sum(weights, axis=-1)
    probs = weights.astype(jnp.bfloat16)
    mixed = jnp.einsum("htu,uhd->thd", probs, value, preferred_element_type=jnp.float32)
    attended = mixed / jnp.transpose(total)[..., None]
    return attended.astype(jnp.bfloat16).reshape(tokens, attn)


def pack_rows(pieces):
    joined = jnp.concatenate(pieces, axis=1)
    eye = jnp.eye(joined.shape[1], dtype=joined.dtype)
    return jnp.einsum("rc,kc->rk", eye, joined, preferred_element_type=joined.dtype)


def project(x, gathered):
    count, cols, _ = gathered.shape
    y = jnp.einsum("tk,sck->tsc", x, gathered, preferred_element_type=jnp.float32)
    return y.reshape(x.shape[0], count * cols)


def per_device(
    frames_in,
    modulation,
    self_proj,
    self_out,
    cross_query,
    cross_keyval,
    cross_out,
    text_bank,
    prompt_pick,
    text_lengths,
):
    count = lax.axis_size("seq")
    frame_rows, pixels, width = frames_in.shape
    attn = self_out.shape[0]
    heads = attn // HEAD_DIM
    scale_q = 1.0 / math.sqrt(HEAD_DIM)
    pix_dev = pixels // count
    frames = frame_rows * count
    text_len = text_bank.shape[1]
    txt_dev = text_len // count

    outs_pair = jnp.concatenate([self_out, cross_out], axis=0)
    sizes = (self_proj.shape[1], cross_keyval.shape[1], cross_query.shape[1], outs_pair.shape[1])
    packed = pack_rows([self_proj, cross_keyval, cross_query, outs_pair])
    gathered = lax.all_gather(packed, "seq", axis=0, tiled=False)
    kv_at = sizes[0]
    q_at = kv_at + sizes[1]
    outs_at = q_at + sizes[2]
    query_g = gathered[:, q_at : q_at + sizes[2], :]
    outs_g = gathered[:, outs_at : outs_at + sizes[3], :]

    tokens = frames_in.astype(jnp.float32)
    normed = (layer_norm(tokens) * (1.0 + modulation[1]) + modulation[0]).astype(jnp.bfloat16)
    send = jnp.concatenate(
        [
            normed.reshape(count, pix_dev, width),
            text_bank[0].reshape(count, txt_dev, width),
        ],
        axis=1,
    )
    recv = lax.all_to_all(send, "seq", 0, 0, tiled=True)
    switched = recv[:, :pix_dev, :]
    pick = prompt_pick[0]
    memory_rows = lax.dynamic_index_in_dim(recv[:, pix_dev:, :], pick, 0, keepdims=False)

    flat_pix = switched.reshape(-1, width)
    both = jnp.concatenate([flat_pix, memory_rows], axis=0)
    lead = -(-(kv_at + sizes[1]) // 16) * 16
    both_out = jnp.einsum(
        "tk,sck->tsc", both, gathered[:, :lead, :], preferred_element_type=jnp.float32
    )
    tok = flat_pix.shape[0]
    qkv = both_out[:tok, :, : sizes[0]].reshape(tok, -1).astype(jnp.bfloat16)
    attended = temporal_attention(qkv, heads, attn, scale_q, pix_dev)

    keyval_rows = both_out[tok:, :, kv_at : kv_at + sizes[1]].reshape(txt_dev, -1).astype(jnp.bfloat16)
    key_rows = head_norm(keyval_rows[:, :attn].astype(jnp.float32), heads).astype(jnp.bfloat16)
    kv_rows = jnp.concatenate([key_rows.reshape(txt_dev, attn), keyval_rows[:, attn:]], axis=1)

    blocks = kv_rows.size // (pix_dev * attn)
    send2 = jnp.concatenate(
        [
            attended.reshape(count, 1, pix_dev * attn),
            jnp.broadcast_to(kv_rows.reshape(1, blocks, pix_dev * attn), (count, blocks, pix_dev * attn)),
        ],
        axis=1,
    )
    recv2 = lax.all_to_all(send2, "seq", 0, 0, tiled=True)
    returned = recv2[:, 0, :].reshape(pixels, attn)
    keyval = recv2[:, 1:, :].reshape(text_len, 2 * attn)

    out_self = outs_g[:, :, :attn].reshape(-1, attn)
    out_cross = outs_g[:, :, attn:].reshape(-1, attn)
    self_term = jnp.einsum("ta,ca->tc", returned, out_self, preferred_element_type=jnp.float32)
    after_self = (tokens.reshape(-1, width) + modulation[2] * self_term).astype(jnp.bfloat16)

    text_key = keyval[:, :attn].reshape(text_len, heads, HEAD_DIM)
    text_value = keyval[:, attn:].reshape(text_len, heads, HEAD_DIM)
    slots = jnp.arange(text_lengths.shape[0], dtype=jnp.int32)
    length = jnp.sum(jnp.where(slots == pick, text_lengths, 0))
    live = jnp.arange(text_len, dtype=jnp.int32) < length
    text_query = project(after_self, query_g)
    text_query = (head_norm(text_query, heads) * scale_q).astype(jnp.bfloat16)
    cross_scores = jnp.einsum(
        "thd,lhd->thl", text_query, text_key, preferred_element_type=jnp.float32
    )
    cross_weights = jnp.where(live, jnp.exp(cross_scores), 0.0)
    cross_total = jnp.sum(cross_weights, axis=-1)
    cross_probs = cross_weights.astype(jnp.bfloat16)
    cross_mix = jnp.einsum(
        "thl,lhd->thd", cross_probs, text_value, preferred_element_type=jnp.float32
    )
    crossed = (cross_mix / cross_total[..., None]).astype(jnp.bfloat16).reshape(-1, attn)
    cross_term = jnp.einsum("ta,ca->tc", crossed, out_cross, preferred_element_type=jnp.float32)
    frames_out = (after_self.astype(jnp.float32) + cross_term).astype(jnp.bfloat16)
    return frames_out.reshape(frame_rows, pixels, width)


def solution(mesh):
    placed = (
        P(("clip", "seq"), None, None),
        P("clip", None),
        P(None, "seq"),
        P(None, "seq"),
        P(None, "seq"),
        P(None, "seq"),
        P(None, "seq"),
        P("seq", None, None),
        P("clip"),
        P(),
    )
    return jax.shard_map(
        per_device,
        mesh=mesh,
        in_specs=placed,
        out_specs=P(("clip", "seq"), None, None),
        check_vma=False,
    )
```

```python
import math

import jax
import jax.numpy as jnp
from jax import lax
from jax.sharding import PartitionSpec as P

HEAD_DIM = 72


EPS = 1e-06


def layer_norm(values):
    mean = jnp.mean(values, axis=-1, keepdims=True)
    centred = values - mean
    spread = jnp.mean(centred * centred, axis=-1, keepdims=True)
    return centred * lax.rsqrt(spread + EPS)


def head_norm(values, heads):
    shaped = values.reshape(values.shape[:-1] + (heads, values.shape[-1] // heads))
    power = jnp.mean(shaped * shaped, axis=-1, keepdims=True)
    return shaped * lax.rsqrt(power + EPS)


def temporal_attention(qkv, heads, attn, scale_q, patches):
    tokens = qkv.shape[0]
    query = (head_norm(qkv[:, :attn].astype(jnp.float32), heads) * scale_q).astype(jnp.bfloat16)
    key = head_norm(qkv[:, attn : 2 * attn].astype(jnp.float32), heads).astype(jnp.bfloat16)
    value = qkv[:, 2 * attn :].reshape(tokens, heads, attn // heads)
    scores = jnp.einsum("thd,uhd->htu", query, key, preferred_element_type=jnp.float32)
    patch = jnp.arange(tokens, dtype=jnp.int32) % patches
    same = patch[:, None] == patch[None, :]
    weights = jnp.where(same, jnp.exp(scores), 0.0)
    total = jnp.sum(weights, axis=-1)
    probs = weights.astype(jnp.bfloat16)
    mixed = jnp.einsum("htu,uhd->thd", probs, value, preferred_element_type=jnp.float32)
    attended = mixed / jnp.transpose(total)[..., None]
    return attended.astype(jnp.bfloat16).reshape(tokens, attn)


def pack_rows(pieces):
    joined = jnp.concatenate(pieces, axis=1)
    eye = jnp.eye(joined.shape[1], dtype=joined.dtype)
    return jnp.einsum("rc,kc->rk", eye, joined, preferred_element_type=joined.dtype)


def project(x, gathered):
    count, cols, _ = gathered.shape
    y = jnp.einsum("tk,sck->tsc", x, gathered, preferred_element_type=jnp.float32)
    return y.reshape(x.shape[0], count * cols)


def per_device(
    frames_in,
    modulation,
    self_proj,
    self_out,
    cross_query,
    cross_keyval,
    cross_out,
    text_bank,
    prompt_pick,
    text_lengths,
):
    count = lax.axis_size("seq")
    frame_rows, pixels, width = frames_in.shape
    attn = self_out.shape[0]
    heads = attn // HEAD_DIM
    scale_q = 1.0 / math.sqrt(HEAD_DIM)
    pix_dev = pixels // count
    frames = frame_rows * count
    text_len = text_bank.shape[1]
    txt_dev = text_len // count

    outs_pair = jnp.concatenate([self_out, cross_out], axis=0)
    sizes = (self_proj.shape[1], cross_keyval.shape[1], cross_query.shape[1], outs_pair.shape[1])
    packed = pack_rows([self_proj, cross_keyval, cross_query, outs_pair])
    gathered = lax.all_gather(packed, "seq", axis=0, tiled=False)
    kv_at = sizes[0]
    q_at = kv_at + sizes[1]
    outs_at = q_at + sizes[2]
    query_g = gathered[:, q_at : q_at + sizes[2], :]
    outs_g = gathered[:, outs_at : outs_at + sizes[3], :]

    tokens = frames_in.astype(jnp.float32)
    normed = (layer_norm(tokens) * (1.0 + modulation[1]) + modulation[0]).astype(jnp.bfloat16)
    send = jnp.concatenate(
        [
            normed.reshape(count, pix_dev, width),
            text_bank[0].reshape(count, txt_dev, width),
        ],
        axis=1,
    )
    recv = lax.all_to_all(send, "seq", 0, 0, tiled=True)
    switched = recv[:, :pix_dev, :]
    pick = prompt_pick[0]
    memory_rows = lax.dynamic_index_in_dim(recv[:, pix_dev:, :], pick, 0, keepdims=False)

    flat_pix = switched.reshape(-1, width)
    q_end = -(-sizes[0] // 16) * 16
    qkv_out = jnp.einsum(
        "tk,sck->tsc", flat_pix, gathered[:, :q_end, :], preferred_element_type=jnp.float32
    )
    tok = flat_pix.shape[0]
    qkv = qkv_out[:, :, : sizes[0]].reshape(tok, -1).astype(jnp.bfloat16)
    attended = temporal_attention(qkv, heads, attn, scale_q, pix_dev)

    kv_lo = kv_at // 16 * 16
    kv_hi = -(-(kv_at + sizes[1]) // 16) * 16
    kv_out = jnp.einsum(
        "tk,sck->tsc", memory_rows, gathered[:, kv_lo:kv_hi, :], preferred_element_type=jnp.float32
    )
    keyval_rows = kv_out[:, :, kv_at - kv_lo : kv_at - kv_lo + sizes[1]].reshape(txt_dev, -1).astype(jnp.bfloat16)
    key_rows = head_norm(keyval_rows[:, :attn].astype(jnp.float32), heads).astype(jnp.bfloat16)
    kv_rows = jnp.concatenate([key_rows.reshape(txt_dev, attn), keyval_rows[:, attn:]], axis=1)

    send2 = jnp.concatenate(
        [
            attended.reshape(count, -1),
            jnp.broadcast_to(kv_rows.reshape(1, -1), (count, txt_dev * 2 * attn)),
        ],
        axis=1,
    )
    recv2 = lax.all_to_all(send2, "seq", 0, 0, tiled=True)
    returned = recv2[:, : pix_dev * attn].reshape(pixels, attn)
    keyval = recv2[:, pix_dev * attn :].reshape(text_len, 2 * attn)

    out_self = outs_g[:, :, :attn].reshape(-1, attn)
    out_cross = outs_g[:, :, attn:].reshape(-1, attn)
    self_term = jnp.einsum("ta,ca->tc", returned, out_self, preferred_element_type=jnp.float32)
    after_self = (tokens.reshape(-1, width) + modulation[2] * self_term).astype(jnp.bfloat16)

    text_key = keyval[:, :attn].reshape(text_len, heads, HEAD_DIM)
    text_value = keyval[:, attn:].reshape(text_len, heads, HEAD_DIM)
    slots = jnp.arange(text_lengths.shape[0], dtype=jnp.int32)
    length = jnp.sum(jnp.where(slots == pick, text_lengths, 0))
    live = jnp.arange(text_len, dtype=jnp.int32) < length
    text_query = project(after_self, query_g)
    text_query = (head_norm(text_query, heads) * scale_q).astype(jnp.bfloat16)
    cross_scores = jnp.einsum(
        "thd,lhd->thl", text_query, text_key, preferred_element_type=jnp.float32
    )
    cross_weights = jnp.where(live, jnp.exp(cross_scores), 0.0)
    cross_total = jnp.sum(cross_weights, axis=-1)
    cross_probs = cross_weights.astype(jnp.bfloat16)
    cross_mix = jnp.einsum(
        "thl,lhd->thd", cross_probs, text_value, preferred_element_type=jnp.float32
    )
    crossed = (cross_mix / cross_total[..., None]).astype(jnp.bfloat16).reshape(-1, attn)
    cross_term = jnp.einsum("ta,ca->tc", crossed, out_cross, preferred_element_type=jnp.float32)
    frames_out = (after_self.astype(jnp.float32) + cross_term).astype(jnp.bfloat16)
    return frames_out.reshape(frame_rows, pixels, width)


def solution(mesh):
    placed = (
        P(("clip", "seq"), None, None),
        P("clip", None),
        P(None, "seq"),
        P(None, "seq"),
        P(None, "seq"),
        P(None, "seq"),
        P(None, "seq"),
        P("seq", None, None),
        P("clip"),
        P(),
    )
    return jax.shard_map(
        per_device,
        mesh=mesh,
        in_specs=placed,
        out_specs=P(("clip", "seq"), None, None),
        check_vma=False,
    )
```

```python
import math

import jax
import jax.numpy as jnp
from jax import lax
from jax.sharding import PartitionSpec as P

HEAD_DIM = 72


EPS = 1e-06


def layer_norm(values):
    mean = jnp.mean(values, axis=-1, keepdims=True)
    centred = values - mean
    spread = jnp.mean(centred * centred, axis=-1, keepdims=True)
    return centred * lax.rsqrt(spread + EPS)


def head_norm(values, heads):
    shaped = values.reshape(values.shape[:-1] + (heads, values.shape[-1] // heads))
    power = jnp.mean(shaped * shaped, axis=-1, keepdims=True)
    return shaped * lax.rsqrt(power + EPS)


def temporal_attention(qkv, heads, attn, scale_q, patches):
    tokens = qkv.shape[0]
    query = (head_norm(qkv[:, :attn].astype(jnp.float32), heads) * scale_q).astype(jnp.bfloat16)
    key = head_norm(qkv[:, attn : 2 * attn].astype(jnp.float32), heads).astype(jnp.bfloat16)
    value = qkv[:, 2 * attn :].reshape(tokens, heads, attn // heads)
    scores = jnp.einsum("thd,uhd->htu", query, key, preferred_element_type=jnp.float32)
    patch = jnp.arange(tokens, dtype=jnp.int32) % patches
    same = patch[:, None] == patch[None, :]
    weights = jnp.where(same, jnp.exp(scores), 0.0)
    total = jnp.sum(weights, axis=-1)
    probs = weights.astype(jnp.bfloat16)
    mixed = jnp.einsum("htu,uhd->thd", probs, value, preferred_element_type=jnp.float32)
    attended = mixed / jnp.transpose(total)[..., None]
    return attended.astype(jnp.bfloat16).reshape(tokens, attn)


def pack_rows(pieces):
    joined = jnp.concatenate(pieces, axis=1)
    eye = jnp.eye(joined.shape[1], dtype=joined.dtype)
    return jnp.einsum("rc,kc->rk", eye, joined, preferred_element_type=joined.dtype)


def project(x, gathered):
    count, cols, _ = gathered.shape
    y = jnp.einsum("tk,sck->tsc", x, gathered, preferred_element_type=jnp.float32)
    return y.reshape(x.shape[0], count * cols)


def per_device(
    frames_in,
    modulation,
    self_proj,
    self_out,
    cross_query,
    cross_keyval,
    cross_out,
    text_bank,
    prompt_pick,
    text_lengths,
):
    count = lax.axis_size("seq")
    frame_rows, pixels, width = frames_in.shape
    attn = self_out.shape[0]
    heads = attn // HEAD_DIM
    scale_q = 1.0 / math.sqrt(HEAD_DIM)
    pix_dev = pixels // count
    frames = frame_rows * count
    text_len = text_bank.shape[1]
    txt_dev = text_len // count

    outs_pair = jnp.concatenate([self_out, cross_out], axis=0)
    sizes = (self_proj.shape[1], cross_keyval.shape[1], cross_query.shape[1], outs_pair.shape[1])
    packed = pack_rows([self_proj, cross_keyval, cross_query, outs_pair])
    gathered = lax.all_gather(packed, "seq", axis=0, tiled=False)
    kv_at = sizes[0]
    q_at = kv_at + sizes[1]
    outs_at = q_at + sizes[2]
    query_g = gathered[:, q_at : q_at + sizes[2], :]
    outs_g = gathered[:, outs_at : outs_at + sizes[3], :]

    tokens = frames_in.astype(jnp.float32)
    normed = (layer_norm(tokens) * (1.0 + modulation[1]) + modulation[0]).astype(jnp.bfloat16)
    send = jnp.concatenate(
        [
            normed.reshape(count, pix_dev, width),
            text_bank[0].reshape(count, txt_dev, width),
        ],
        axis=1,
    )
    recv = lax.all_to_all(send, "seq", 0, 0, tiled=True)
    switched = recv[:, :pix_dev, :]
    pick = prompt_pick[0]
    memory_rows = lax.dynamic_index_in_dim(recv[:, pix_dev:, :], pick, 0, keepdims=False)

    flat_pix = switched.reshape(-1, width)
    q_end = -(-sizes[0] // 16) * 16
    qkv_out = jnp.einsum(
        "tk,sck->tsc", flat_pix, gathered[:, :q_end, :], preferred_element_type=jnp.float32
    )
    tok = flat_pix.shape[0]
    qkv = qkv_out[:, :, : sizes[0]].reshape(tok, -1).astype(jnp.bfloat16)
    attended = temporal_attention(qkv, heads, attn, scale_q, pix_dev)

    kv_lo = kv_at // 16 * 16
    kv_hi = -(-(kv_at + sizes[1]) // 16) * 16
    kv_out = jnp.einsum(
        "sck,tk->sct", gathered[:, kv_lo:kv_hi, :], memory_rows, preferred_element_type=jnp.float32
    )
    kv_out = kv_out[:, kv_at - kv_lo : kv_at - kv_lo + sizes[1], :].astype(jnp.bfloat16)
    keyval_rows = jnp.transpose(kv_out, (2, 0, 1)).reshape(txt_dev, -1)
    key_rows = head_norm(keyval_rows[:, :attn].astype(jnp.float32), heads).astype(jnp.bfloat16)
    kv_rows = jnp.concatenate([key_rows.reshape(txt_dev, attn), keyval_rows[:, attn:]], axis=1)

    send2 = jnp.concatenate(
        [
            attended.reshape(count, -1),
            jnp.broadcast_to(kv_rows.reshape(1, -1), (count, txt_dev * 2 * attn)),
        ],
        axis=1,
    )
    recv2 = lax.all_to_all(send2, "seq", 0, 0, tiled=True)
    returned = recv2[:, : pix_dev * attn].reshape(pixels, attn)
    keyval = recv2[:, pix_dev * attn :].reshape(text_len, 2 * attn)

    out_self = outs_g[:, :, :attn].reshape(-1, attn)
    out_cross = outs_g[:, :, attn:].reshape(-1, attn)
    self_term = jnp.einsum("ta,ca->tc", returned, out_self, preferred_element_type=jnp.float32)
    after_self = (tokens.reshape(-1, width) + modulation[2] * self_term).astype(jnp.bfloat16)

    text_key = keyval[:, :attn].reshape(text_len, heads, HEAD_DIM)
    text_value = keyval[:, attn:].reshape(text_len, heads, HEAD_DIM)
    slots = jnp.arange(text_lengths.shape[0], dtype=jnp.int32)
    length = jnp.sum(jnp.where(slots == pick, text_lengths, 0))
    live = jnp.arange(text_len, dtype=jnp.int32) < length
    text_query = project(after_self, query_g)
    text_query = (head_norm(text_query, heads) * scale_q).astype(jnp.bfloat16)
    cross_scores = jnp.einsum(
        "thd,lhd->thl", text_query, text_key, preferred_element_type=jnp.float32
    )
    cross_weights = jnp.where(live, jnp.exp(cross_scores), 0.0)
    cross_total = jnp.sum(cross_weights, axis=-1)
    cross_probs = cross_weights.astype(jnp.bfloat16)
    cross_mix = jnp.einsum(
        "thl,lhd->thd", cross_probs, text_value, preferred_element_type=jnp.float32
    )
    crossed = (cross_mix / cross_total[..., None]).astype(jnp.bfloat16).reshape(-1, attn)
    cross_term = jnp.einsum("ta,ca->tc", crossed, out_cross, preferred_element_type=jnp.float32)
    frames_out = (after_self.astype(jnp.float32) + cross_term).astype(jnp.bfloat16)
    return frames_out.reshape(frame_rows, pixels, width)


def solution(mesh):
    placed = (
        P(("clip", "seq"), None, None),
        P("clip", None),
        P(None, "seq"),
        P(None, "seq"),
        P(None, "seq"),
        P(None, "seq"),
        P(None, "seq"),
        P("seq", None, None),
        P("clip"),
        P(),
    )
    return jax.shard_map(
        per_device,
        mesh=mesh,
        in_specs=placed,
        out_specs=P(("clip", "seq"), None, None),
        check_vma=False,
    )
```
